256 devices in a mesh: run: 2 (over core), ctx: 32 (over x, z), head: 4 (over y).
Axes of the slice: x: 4, y: 4, z: 8, core: 2. Of those that a mesh axis runs over, the one named last changes fastest.
Arguments:
- inner_tokens: bfloat16 [131072, 5120], P(('run', 'ctx', 'head')), parts along dimension 0, may hold values from -6 to 6
- state_inputs: bfloat16 [131072, 256], P(('run', 'ctx', 'head')), parts along dimension 0, may hold values from -6 to 6
- step_raw: bfloat16 [131072, 80], P(('run', 'ctx', 'head')), parts along dimension 0, may hold values from -3 to 24
- conv_inner: float32 [5, 5120], P(None, 'head'), may hold values from -3 to 3
- conv_state: float32 [5, 256], replicated, may hold values from -3 to 3
- head_rates: float32 [4, 80], P('run', 'head'), parts along dimension 0, may hold values from -15 to 4
- skip_gain: float32 [80], P('head'), may hold values from 0.5 to 1.5
Outputs:
- mixed: bfloat16 [131072, 5120], P(('run', 'ctx', 'head')), parts along dimension 0
The draws below stay inside these ranges and needn't reach their ends.
There are 2 independent parts, one for each index of `run`. The reference program is written for one: setup_inputs(seed, part) draws one part's arguments, and reference() takes and returns one part's arrays. A program takes and returns all parts, laid end to end along the dimension named above; an argument that names none is the same for every part. Nothing has to cross between parts.
All inputs are finite; a program needn't handle non-finite values.
Results may differ from the reference program's by a relative error of at most 0.009.
Values may be sent and summed in bfloat16 or wider, within the bound.
No kernel may reach another device: no remote copies, remote signals or barrier semaphores. Data moves between devices by JAX's collectives and lax.ppermute only.
A program may use at most 192 MiB of HBM per device.

```python
import jax
import jax.numpy as jnp
from jax import lax

HEADS = 80
HEAD_DIM = 64
STATE = 128
KERNEL = 4
SPAN = 256
INNER = 5120
SEQ = 65536


def head_profile(key):
    first, second, third = jax.random.split(jax.random.fold_in(key, 17), 3)
    share = 0.5
    quick = jax.random.bernoulli(first, share, (HEADS,))
    jitter_step = jax.random.uniform(second, (HEADS,), jnp.float32, 0.5, 2.0)
    jitter_rate = jax.random.uniform(third, (HEADS,), jnp.float32, 0.6, 1.6)
    quick_step = 0.003 * jitter_step
    slow_step = 3.0 / SEQ * jitter_step
    chosen_step = jnp.where(quick, quick_step, slow_step)
    quick_rate = 0.025 / quick_step * jitter_rate
    slow_rate = 0.4 / (SEQ * slow_step) * jitter_rate
    selected_rate = jnp.where(quick, quick_rate, slow_rate)
    return (quick, chosen_step, selected_rate)


def draw_head_rates(key, part):
    quick, chosen_step, selected_rate = head_profile(key)
    row_bias_vector = jnp.log(jnp.expm1(chosen_step))
    return jnp.stack([row_bias_vector, jnp.log(selected_rate)], axis=0).astype(jnp.float32)


def draw_step_raw(key, part):
    quick, chosen_step, selected_rate = head_profile(key)
    row_bias_vector = jnp.log(jnp.expm1(chosen_step))
    noise_key, block_key, offset_key, gap_key, loss_key = jax.random.split(jax.random.fold_in(key, 29), 5)
    base = 0.5 * jax.random.truncated_normal(noise_key, -6.0, 6.0, (SEQ, HEADS), jnp.float32)
    positions = jnp.arange(SEQ, dtype=jnp.int32)[:, None]
    block_start = jax.random.randint(block_key, (2, HEADS), 0, SEQ // SPAN) * SPAN
    first_place = block_start + jax.random.randint(offset_key, (2, HEADS), 0, SPAN // 2)
    second_place = first_place + jax.random.randint(gap_key, (2, HEADS), 1, SPAN // 2 + 1)
    dropped_flags = jax.random.uniform(loss_key, (4, HEADS), jnp.float32, 0.22, 0.4)
    places = jnp.concatenate([first_place, second_place], axis=0)
    bursty = jnp.logical_not(quick)
    unscaled_values = base
    for selector_index in range(4):
        spike_value = jnp.log(jnp.expm1(dropped_flags[selector_index] / selected_rate)) - row_bias_vector
        event_mask = jnp.logical_and(positions == places[selector_index][None, :], bursty[None, :])
        unscaled_values = jnp.where(event_mask, spike_value[None, :], unscaled_values)
    return unscaled_values.astype(jnp.bfloat16)


def segment_offsets(key):
    segment_count = SEQ // 64 + 1
    shared_key, other_key, mapping_key = jax.random.split(jax.random.fold_in(key, 41), 3)
    shared = jax.random.uniform(shared_key, (segment_count, STATE), jnp.float32, -2.0, 2.0)
    c_offsets = jax.random.uniform(other_key, (segment_count, STATE), jnp.float32, -2.0, 2.0)
    head_keys = jax.random.split(mapping_key, HEADS)
    mapping = jax.vmap(lambda single: jax.random.permutation(single, STATE)[:HEAD_DIM])(head_keys).reshape(HEADS * HEAD_DIM).astype(jnp.int32)
    segment = (jnp.arange(SEQ, dtype=jnp.int32) // 64).astype(jnp.int32)
    return (shared, c_offsets, mapping, segment)


def token_noise(key, columns):
    return jax.random.truncated_normal(key, -4.0, 4.0, (SEQ, columns), jnp.float32)


def draw_inner_tokens(key, part):
    shared, c_offsets, mapping, segment = segment_offsets(key)
    noise = token_noise(jax.random.fold_in(key, 53), HEADS * HEAD_DIM)
    per_segment = jnp.take(shared, mapping, axis=1)
    per_token = jnp.take(per_segment, segment, axis=0)
    return jnp.clip(noise + per_token, -6.0, 6.0).astype(jnp.bfloat16)


def draw_state_inputs(key, part):
    shared, c_offsets, mapping, segment = segment_offsets(key)
    noise = token_noise(jax.random.fold_in(key, 59), 2 * STATE)
    offsets = jnp.concatenate([jnp.take(shared, segment, axis=0), jnp.take(c_offsets, segment, axis=0)], axis=1)
    return jnp.clip(noise + offsets, -6.0, 6.0).astype(jnp.bfloat16)


def shard_levels(rng, shape, cuts, low, high):
    level = 1.0
    for axis_at, parts in cuts:
        heights = jax.random.uniform(jax.random.fold_in(jax.random.fold_in(rng, 6), axis_at), (parts,), jnp.float32, low / len(cuts), high / len(cuts))
        level = level * jnp.repeat(jnp.exp(heights), shape[axis_at] // parts).reshape((-1,) + (1,) * (len(shape) - 1 - axis_at))
    return level


def centred(key, extent, scale, reach, cuts=(), kind=jnp.bfloat16):
    loudness = shard_levels(key, extent, cuts, -0.22, 0.18) if cuts else 1.0
    drawn = jax.random.normal(key, extent, jnp.float32) * scale * loudness
    return jnp.minimum(jnp.maximum(drawn, -reach), reach).astype(kind)


def setup_inputs(seed: int = 0, part: int = 0) -> dict:
    arg_keys = jax.random.split(jax.random.key(seed), 8)
    part_splits = jax.random.split(jax.random.fold_in(arg_keys[7], part), 8)
    return {
        "inner_tokens": draw_inner_tokens(jax.random.fold_in(jax.random.fold_in(arg_keys[7], part), 71), part),
        "state_inputs": draw_state_inputs(jax.random.fold_in(jax.random.fold_in(arg_keys[7], part), 71), part),
        "step_raw": draw_step_raw(jax.random.fold_in(jax.random.fold_in(arg_keys[7], part), 71), part),
        "conv_inner": centred(arg_keys[3], (KERNEL + 1, INNER), 0.5, 3.0, ((1, 4),), jnp.float32),
        "conv_state": centred(arg_keys[4], (KERNEL + 1, 2 * STATE), 0.5, 3.0, (), jnp.float32),
        "head_rates": draw_head_rates(jax.random.fold_in(jax.random.fold_in(arg_keys[7], part), 71), part),
        "skip_gain": jnp.clip(0.5 + 1.0 * jax.random.uniform(arg_keys[6], (HEADS,), jnp.float32) ** shard_levels(arg_keys[6], (HEADS,), ((0, 4),), -0.2, 0.2), 0.5, 1.5),
    }


def silu_conv(signal, kernel_taps):
    length = signal.shape[0]
    channels = signal.shape[1]
    padded = jnp.concatenate([jnp.zeros((KERNEL - 1, channels), jnp.float32), signal.astype(jnp.float32)], axis=0)
    summed = jnp.zeros((length, channels), jnp.float32) + kernel_taps[KERNEL][None, :]
    for offset in range(KERNEL):
        summed = summed + kernel_taps[offset][None, :] * padded[offset:offset + length]
    return jax.nn.silu(summed).astype(jnp.bfloat16)


def block_terms(carry_state, pieces):
    c_block, b_block, u_block, decay_block = pieces
    cumulative = jnp.cumsum(decay_block, axis=0)
    across = cumulative.T
    inner_scores = jnp.dot(c_block, b_block.T, preferred_element_type=jnp.float32)
    spread = across[:, :, None] - across[:, None, :]
    places = jnp.arange(c_block.shape[0])
    causal = places[:, None] >= places[None, :]
    mixing = (inner_scores[None] * jnp.exp(jnp.where(causal[None], spread, -jnp.inf))).astype(jnp.bfloat16)
    local_terms = jnp.einsum("hts,shp->thp", mixing.astype(jnp.float32), u_block.astype(jnp.float32), precision=lax.Precision.HIGHEST)
    carried = jnp.exp(cumulative)[:, :, None] * jnp.einsum("tn,hpn->thp", c_block.astype(jnp.float32), carry_state, precision=lax.Precision.HIGHEST)
    ending = cumulative[-1]
    weights = jnp.exp(ending[None, :] - cumulative)
    scaled = weights[:, :, None] * u_block.astype(jnp.float32)
    new_state = jnp.exp(ending)[:, None, None] * carry_state + jnp.einsum("shp,sn->hpn", scaled, b_block.astype(jnp.float32), precision=lax.Precision.HIGHEST)
    return new_state, local_terms + carried


def reference(inner_tokens, state_inputs, step_raw, conv_inner, conv_state, head_rates, skip_gain):
    inner_conv = silu_conv(inner_tokens, conv_inner)
    state_conv = silu_conv(state_inputs, conv_state)
    b_rows = state_conv[:, :STATE]
    c_rows = state_conv[:, STATE:]
    step_size = jax.nn.softplus(step_raw.astype(jnp.float32) + head_rates[0][None, :])
    log_decay = -step_size * jnp.exp(head_rates[1])[None, :]
    x_heads = inner_conv.reshape(SEQ, HEADS, HEAD_DIM).astype(jnp.float32)
    inputs = (x_heads * step_size[:, :, None]).astype(jnp.bfloat16)
    block_count = SEQ // SPAN
    start_state = jnp.zeros((HEADS, HEAD_DIM, STATE), jnp.float32)
    final_state, outputs = lax.scan(block_terms, start_state, (c_rows.reshape(block_count, SPAN, STATE), b_rows.reshape(block_count, SPAN, STATE), inputs.reshape(block_count, SPAN, HEADS, HEAD_DIM), log_decay.reshape(block_count, SPAN, HEADS)))
    summed = outputs.reshape(SEQ, HEADS, HEAD_DIM) + skip_gain[None, :, None] * x_heads
    return summed.astype(jnp.bfloat16).reshape(SEQ, INNER)
```

```python
import jax
import jax.numpy as jnp
from jax import lax
from jax.sharding import PartitionSpec as P

KERNEL = 4
SPAN = 256


def from_behind(value, axis, by):
    length = lax.axis_size(axis)
    pairs = [(i, i + by) for i in range(length) if 0 <= i + by < length]
    return lax.ppermute(value, axis, pairs)


def silu_conv(signal, previous_rows, kernel_taps):
    length = signal.shape[0]
    channels = signal.shape[1]
    padded = jnp.concatenate(
        [previous_rows.astype(jnp.float32), signal.astype(jnp.float32)], axis=0
    )
    summed = jnp.zeros((length, channels), jnp.float32) + kernel_taps[KERNEL][None, :]
    for offset in range(KERNEL):
        summed = summed + kernel_taps[offset][None, :] * padded[offset : offset + length]
    return jax.nn.silu(summed).astype(jnp.bfloat16)


def relay_states(decay, state, axis):
    length = lax.axis_size(axis)
    decay = from_behind(decay, axis, 1)
    state = from_behind(state, axis, 1)
    shift = 1
    while shift < length:
        decay_in = from_behind(decay, axis, shift)
        state_in = from_behind(state, axis, shift)
        state = decay[:, None, None] * state_in + state
        decay = decay * decay_in
        shift *= 2
    return state


def per_device(inner_tokens, state_inputs, step_raw, conv_inner, conv_state, head_rates, skip_gain):
    x_local, step_local = (
        lax.all_to_all(inner_tokens, "head", split_axis=1, concat_axis=0, tiled=True),
        lax.all_to_all(step_raw, "head", split_axis=1, concat_axis=0, tiled=True),
    )
    context = x_local.shape[0]
    channels = x_local.shape[1]
    heads_local = head_rates.shape[1]
    head_width = channels // heads_local
    margin_rows = KERNEL - 1
    state_whole = lax.all_gather(state_inputs, "head", axis=0, tiled=True)
    edge_rows = jnp.concatenate(
        [x_local[context - margin_rows :], state_whole[context - margin_rows :]], axis=1
    )
    previous_rows = from_behind(edge_rows, "ctx", 1)
    x_previous = previous_rows[:, :channels]
    state_conv = silu_conv(state_whole, previous_rows[:, channels:], conv_state)
    inner_conv = silu_conv(x_local, x_previous, conv_inner)
    state_width = state_conv.shape[1] // 2
    b_rows = state_conv[:, :state_width]
    c_rows = state_conv[:, state_width:]
    step_size = jax.nn.softplus(step_local.astype(jnp.float32) + head_rates[0][None, :])
    log_decay = -step_size * jnp.exp(head_rates[1])[None, :]
    x_heads = inner_conv.reshape(context, heads_local, head_width)
    inputs = (x_heads.astype(jnp.float32) * step_size[:, :, None]).astype(jnp.bfloat16)
    block_count = context // SPAN

    c_blocks = c_rows.reshape(block_count, SPAN, state_width)
    b_blocks = b_rows.reshape(block_count, SPAN, state_width)
    u_blocks = inputs.reshape(block_count, SPAN, heads_local, head_width)
    cumulative = jnp.cumsum(log_decay.reshape(block_count, SPAN, heads_local), axis=1)
    ending = cumulative[:, -1, :]

    weights = jnp.exp(ending[:, None, :] - cumulative)
    scaled = weights[:, :, :, None] * u_blocks.astype(jnp.float32)
    block_states = jnp.einsum(
        "bshp,bsn->bhpn", scaled, b_blocks.astype(jnp.float32), precision=lax.Precision.HIGHEST
    )
    block_decay = jnp.exp(ending)
    entering = []
    running = jnp.zeros_like(block_states[0])
    decay_before = []
    running_decay = jnp.ones_like(block_decay[0])
    for k in range(block_count):
        entering.append(running)
        decay_before.append(running_decay)
        running = block_decay[k][:, None, None] * running + block_states[k]
        running_decay = running_decay * block_decay[k]
    incoming = relay_states(running_decay, running, "ctx")

    inner_scores = jnp.einsum("btn,bsn->bts", c_blocks, b_blocks, preferred_element_type=jnp.float32)
    across = cumulative.transpose(0, 2, 1)
    spread = across[:, :, :, None] - across[:, :, None, :]
    places = jnp.arange(SPAN)
    causal = places[:, None] >= places[None, :]
    mixing = (
        inner_scores[:, None] * jnp.exp(jnp.where(causal[None, None], spread, -jnp.inf))
    ).astype(jnp.bfloat16)
    local_terms = jnp.einsum(
        "bhts,bshp->bthp", mixing, u_blocks, preferred_element_type=jnp.float32
    )

    entering_all = jnp.stack(entering) + jnp.stack(decay_before)[:, :, None, None] * incoming[None]
    carried = jnp.exp(cumulative)[:, :, :, None] * jnp.einsum(
        "btn,bhpn->bthp",
        c_blocks.astype(jnp.float32),
        entering_all,
        precision=lax.Precision.HIGHEST,
    )
    summed = (
        (local_terms + carried).reshape(context, heads_local, head_width)
        + skip_gain[None, :, None] * x_heads.astype(jnp.float32)
    )
    regrouped = summed.astype(jnp.bfloat16).reshape(context, channels)
    return lax.all_to_all(regrouped, "head", split_axis=0, concat_axis=1, tiled=True)


def solution(mesh):
    return jax.shard_map(
        per_device,
        mesh=mesh,
        in_specs=(
            P(("run", "ctx", "head"), None),
            P(("run", "ctx", "head"), None),
            P(("run", "ctx", "head"), None),
            P(None, "head"),
            P(),
            P("run", "head"),
            P("head"),
        ),
        out_specs=P(("run", "ctx", "head"), None),
        check_vma=False,
    )
```

```python
import jax
import jax.numpy as jnp
from jax import lax
from jax.sharding import PartitionSpec as P

KERNEL = 4
SPAN = 256


def from_behind(value, axis, by):
    length = lax.axis_size(axis)
    pairs = [(i, i + by) for i in range(length) if 0 <= i + by < length]
    return lax.ppermute(value, axis, pairs)


def silu_conv(signal, previous_rows, kernel_taps):
    length = signal.shape[0]
    channels = signal.shape[1]
    padded = jnp.concatenate(
        [previous_rows.astype(jnp.float32), signal.astype(jnp.float32)], axis=0
    )
    summed = jnp.zeros((length, channels), jnp.float32) + kernel_taps[KERNEL][None, :]
    for offset in range(KERNEL):
        summed = summed + kernel_taps[offset][None, :] * padded[offset : offset + length]
    return jax.nn.silu(summed).astype(jnp.bfloat16)


def relay_states(decay, state, axis):
    length = lax.axis_size(axis)
    heads = decay.shape[0]
    size = state.size
    pad = (-heads) % 128

    def pack(d, s):
        return jnp.concatenate([s.reshape(-1), jnp.pad(d, (0, pad))])

    def unpack(payload):
        return payload[size : size + heads], payload[:size].reshape(heads, -1)

    flat_state = state.reshape(heads, -1)
    arrived = from_behind(pack(decay, flat_state), axis, 1)
    excl_decay, excl_state = unpack(arrived)
    incl_state = decay[:, None] * excl_state + flat_state
    incl_decay = decay * excl_decay
    shift = 2
    while shift < length:
        got_decay, got_state = unpack(from_behind(pack(incl_decay, incl_state), axis, shift))
        excl_state = excl_decay[:, None] * got_state + excl_state
        incl_state = incl_decay[:, None] * got_state + incl_state
        excl_decay = excl_decay * got_decay
        incl_decay = incl_decay * got_decay
        shift *= 2
    return excl_state.reshape(state.shape)


def per_device(inner_tokens, state_inputs, step_raw, conv_inner, conv_state, head_rates, skip_gain):
    x_local, step_local = (
        lax.all_to_all(inner_tokens, "head", split_axis=1, concat_axis=0, tiled=True),
        lax.all_to_all(step_raw, "head", split_axis=1, concat_axis=0, tiled=True),
    )
    context = x_local.shape[0]
    channels = x_local.shape[1]
    heads_local = head_rates.shape[1]
    head_width = channels // heads_local
    margin_rows = KERNEL - 1
    state_whole = lax.all_gather(state_inputs, "head", axis=0, tiled=True)
    edge_rows = jnp.concatenate(
        [x_local[context - margin_rows :], state_whole[context - margin_rows :]], axis=1
    )
    previous_rows = from_behind(edge_rows, "ctx", 1)
    x_previous = previous_rows[:, :channels]
    state_conv = silu_conv(state_whole, previous_rows[:, channels:], conv_state)
    inner_conv = silu_conv(x_local, x_previous, conv_inner)
    state_width = state_conv.shape[1] // 2
    b_rows = state_conv[:, :state_width]
    c_rows = state_conv[:, state_width:]
    step_size = jax.nn.softplus(step_local.astype(jnp.float32) + head_rates[0][None, :])
    log_decay = -step_size * jnp.exp(head_rates[1])[None, :]
    x_heads = inner_conv.reshape(context, heads_local, head_width)
    inputs = (x_heads.astype(jnp.float32) * step_size[:, :, None]).astype(jnp.bfloat16)
    block_count = context // SPAN

    c_blocks = c_rows.reshape(block_count, SPAN, state_width)
    b_blocks = b_rows.reshape(block_count, SPAN, state_width)
    u_blocks = inputs.reshape(block_count, SPAN, heads_local, head_width)
    cumulative = jnp.cumsum(log_decay.reshape(block_count, SPAN, heads_local), axis=1)
    ending = cumulative[:, -1, :]

    weights = jnp.exp(ending[:, None, :] - cumulative)
    scaled = weights[:, :, :, None] * u_blocks.astype(jnp.float32)
    block_states = jnp.einsum(
        "bshp,bsn->bhpn", scaled, b_blocks.astype(jnp.float32), precision=lax.Precision.HIGHEST
    )
    block_decay = jnp.exp(ending)
    entering = []
    running = jnp.zeros_like(block_states[0])
    decay_before = []
    running_decay = jnp.ones_like(block_decay[0])
    for k in range(block_count):
        entering.append(running)
        decay_before.append(running_decay)
        running = block_decay[k][:, None, None] * running + block_states[k]
        running_decay = running_decay * block_decay[k]
    incoming = relay_states(running_decay, running, "ctx")

    inner_scores = jnp.einsum("btn,bsn->bts", c_blocks, b_blocks, preferred_element_type=jnp.float32)
    across = cumulative.transpose(0, 2, 1)
    spread = across[:, :, :, None] - across[:, :, None, :]
    places = jnp.arange(SPAN)
    causal = places[:, None] >= places[None, :]
    mixing = (
        inner_scores[:, None] * jnp.exp(jnp.where(causal[None, None], spread, -jnp.inf))
    ).astype(jnp.bfloat16)
    local_terms = jnp.einsum(
        "bhts,bshp->bthp", mixing, u_blocks, preferred_element_type=jnp.float32
    )
    c_float = c_blocks.astype(jnp.float32)
    entering_intra = jnp.stack(entering).reshape(block_count, channels, state_width)
    carried_intra = jnp.einsum(
        "btn,bkn->btk", c_float, entering_intra, precision=lax.Precision.HIGHEST
    ).reshape(block_count, SPAN, heads_local, head_width)
    decay_in = jnp.exp(cumulative)
    known = (
        local_terms
        + decay_in[:, :, :, None] * carried_intra
        + skip_gain[None, None, :, None] * u_x(x_heads, block_count)
    )

    carried_in = jnp.einsum(
        "btn,kn->btk", c_float, incoming.reshape(channels, state_width), precision=lax.Precision.HIGHEST
    ).reshape(block_count, SPAN, heads_local, head_width)
    factor = decay_in * jnp.stack(decay_before)[:, None, :]
    summed = known + factor[:, :, :, None] * carried_in
    regrouped = summed.astype(jnp.bfloat16).reshape(context, channels)
    return lax.all_to_all(regrouped, "head", split_axis=0, concat_axis=1, tiled=True)


def u_x(x_heads, block_count):
    return x_heads.astype(jnp.float32).reshape(block_count, SPAN, *x_heads.shape[1:])


def solution(mesh):
    return jax.shard_map(
        per_device,
        mesh=mesh,
        in_specs=(
            P(("run", "ctx", "head"), None),
            P(("run", "ctx", "head"), None),
            P(("run", "ctx", "head"), None),
            P(None, "head"),
            P(),
            P("run", "head"),
            P("head"),
        ),
        out_specs=P(("run", "ctx", "head"), None),
        check_vma=False,
    )
```

```python
import jax
import jax.numpy as jnp
from jax import lax
from jax.sharding import PartitionSpec as P


KERNEL = 4
SPAN = 256


def from_behind(value, axis, by):
    length = lax.axis_size(axis)
    pairs = [(i, i + by) for i in range(length) if 0 <= i + by < length]
    return lax.ppermute(value, axis, pairs)


def silu_conv(signal, previous_rows, kernel_taps):
    length = signal.shape[0]
    channels = signal.shape[1]
    padded = jnp.concatenate(
        [previous_rows.astype(jnp.float32), signal.astype(jnp.float32)], axis=0
    )
    summed = jnp.zeros((length, channels), jnp.float32) + kernel_taps[KERNEL][None, :]
    for offset in range(KERNEL):
        summed = summed + kernel_taps[offset][None, :] * padded[offset : offset + length]
    return jax.nn.silu(summed).astype(jnp.bfloat16)


def relay_states(decay, state, axis):
    length = lax.axis_size(axis)
    heads = decay.shape[0]
    size = state.size
    pad = (-heads) % 128

    def pack(d, s):
        return jnp.concatenate([s.reshape(-1), jnp.pad(d, (0, pad))])

    def unpack(payload):
        return payload[size : size + heads], payload[:size].reshape(heads, -1)

    flat_state = state.reshape(heads, -1)
    arrived = from_behind(pack(decay, flat_state), axis, 1)
    excl_decay, excl_state = unpack(arrived)
    incl_state = decay[:, None] * excl_state + flat_state
    incl_decay = decay * excl_decay
    shift = 2
    while shift < length:
        sent = from_behind(pack(incl_decay, incl_state), axis, shift)
        got_decay, got_state = unpack(sent)
        excl_state = excl_decay[:, None] * got_state + excl_state
        incl_state = incl_decay[:, None] * got_state + incl_state
        excl_decay = excl_decay * got_decay
        incl_decay = incl_decay * got_decay
        shift *= 2
    return excl_state.reshape(state.shape)


def per_device(inner_tokens, state_inputs, step_raw, conv_inner, conv_state, head_rates, skip_gain):
    x_local, step_local = (
        lax.all_to_all(inner_tokens, "head", split_axis=1, concat_axis=0, tiled=True),
        lax.all_to_all(step_raw, "head", split_axis=1, concat_axis=0, tiled=True),
    )
    context = x_local.shape[0]
    channels = x_local.shape[1]
    heads_local = head_rates.shape[1]
    head_width = channels // heads_local
    margin_rows = KERNEL - 1
    state_whole = lax.all_gather(state_inputs, "head", axis=0, tiled=True)
    edge_rows = jnp.concatenate(
        [x_local[context - margin_rows :], state_whole[context - margin_rows :]], axis=1
    )
    previous_rows = from_behind(edge_rows, "ctx", 1)
    x_previous = previous_rows[:, :channels]
    state_conv = silu_conv(state_whole, previous_rows[:, channels:], conv_state)
    inner_conv = silu_conv(x_local, x_previous, conv_inner)
    state_width = state_conv.shape[1] // 2
    b_rows = state_conv[:, :state_width]
    c_rows = state_conv[:, state_width:]
    step_size = jax.nn.softplus(step_local.astype(jnp.float32) + head_rates[0][None, :])
    log_decay = -step_size * jnp.exp(head_rates[1])[None, :]
    x_heads = inner_conv.reshape(context, heads_local, head_width)
    inputs = (x_heads.astype(jnp.float32) * step_size[:, :, None]).astype(jnp.bfloat16)
    block_count = context // SPAN

    c_blocks = c_rows.reshape(block_count, SPAN, state_width)
    b_blocks = b_rows.reshape(block_count, SPAN, state_width)
    u_blocks = inputs.reshape(block_count, SPAN, heads_local, head_width)
    cumulative = jnp.cumsum(log_decay.reshape(block_count, SPAN, heads_local), axis=1)
    ending = cumulative[:, -1, :]

    weights = jnp.exp(ending[:, None, :] - cumulative)
    scaled = weights[:, :, :, None] * u_blocks.astype(jnp.float32)
    block_states = jnp.einsum(
        "bshp,bsn->bhpn", scaled, b_blocks.astype(jnp.float32), precision=lax.Precision.HIGHEST
    )
    block_decay = jnp.exp(ending)
    entering = []
    running = jnp.zeros_like(block_states[0])
    running_decay = jnp.ones_like(block_decay[0])
    for k in range(block_count):
        entering.append(running)
        running = block_decay[k][:, None, None] * running + block_states[k]
        running_decay = running_decay * block_decay[k]
    incoming = relay_states(running_decay, running, "ctx")

    inner_scores = jnp.einsum("btn,bsn->bts", c_blocks, b_blocks, preferred_element_type=jnp.float32)
    across = cumulative.transpose(0, 2, 1)
    spread = across[:, :, :, None] - across[:, :, None, :]
    places = jnp.arange(SPAN)
    causal = places[:, None] >= places[None, :]
    mixing = (
        inner_scores[:, None] * jnp.exp(jnp.where(causal[None, None], spread, -jnp.inf))
    ).astype(jnp.bfloat16)
    local_terms = jnp.einsum(
        "bhts,bshp->bthp", mixing, u_blocks, preferred_element_type=jnp.float32
    )
    c_float = c_blocks.astype(jnp.float32)
    entering_intra = jnp.stack(entering).reshape(block_count, channels, state_width)
    carried_intra = jnp.einsum(
        "btn,bkn->btk", c_float, entering_intra, precision=lax.Precision.HIGHEST
    ).reshape(block_count, SPAN, heads_local, head_width)
    decay_in = jnp.exp(cumulative)
    known = (
        local_terms
        + decay_in[:, :, :, None] * carried_intra
        + skip_gain[None, None, :, None] * u_x(x_heads, block_count)
    )

    partial = known.astype(jnp.bfloat16).reshape(context, channels)
    partial_tokens = lax.all_to_all(partial, "head", split_axis=0, concat_axis=1, tiled=True)

    tokens = inner_tokens.shape[0]
    group = lax.axis_index("head")
    rates_all = lax.all_gather(head_rates, "head", axis=1, tiled=True)
    step_tokens = jax.nn.softplus(step_raw.astype(jnp.float32) + rates_all[0][None, :])
    decay_tokens = -step_tokens * jnp.exp(rates_all[1])[None, :]
    cumulative_tokens = jnp.cumsum(decay_tokens.reshape(tokens // SPAN, SPAN, -1), axis=1)
    ends_all = lax.all_gather(cumulative_tokens[:, -1, :], "head", axis=0, tiled=True)
    exps_all = jnp.exp(ends_all)
    before_all = []
    running_decay = jnp.ones_like(exps_all[0])
    for k in range(exps_all.shape[0]):
        before_all.append(running_decay)
        running_decay = running_decay * exps_all[k]
    before_own = lax.dynamic_slice_in_dim(
        jnp.stack(before_all), group * (tokens // SPAN), tokens // SPAN, axis=0
    )
    factor_tokens = (jnp.exp(cumulative_tokens) * before_own[:, None, :]).reshape(tokens, -1)
    c_tokens = lax.dynamic_slice_in_dim(c_rows, group * tokens, tokens, axis=0).astype(jnp.float32)
    incoming_all = lax.all_gather(incoming, "head", axis=0, tiled=True)
    carried_in = jnp.einsum(
        "tn,kn->tk",
        c_tokens,
        incoming_all.reshape(-1, state_width),
        precision=lax.Precision.HIGHEST,
    ).reshape(tokens, factor_tokens.shape[1], head_width)
    summed = partial_tokens.astype(jnp.float32).reshape(carried_in.shape) + (
        factor_tokens[:, :, None] * carried_in
    )
    return summed.astype(jnp.bfloat16).reshape(tokens, -1)


def u_x(x_heads, block_count):
    return x_heads.astype(jnp.float32).reshape(block_count, SPAN, *x_heads.shape[1:])


def solution(mesh):
    return jax.shard_map(
        per_device,
        mesh=mesh,
        in_specs=(
            P(("run", "ctx", "head"), None),
            P(("run", "ctx", "head"), None),
            P(("run", "ctx", "head"), None),
            P(None, "head"),
            P(),
            P("run", "head"),
            P("head"),
        ),
        out_specs=P(("run", "ctx", "head"), None),
        check_vma=False,
    )
```

```python
import jax
import jax.numpy as jnp
from jax import lax
from jax.sharding import PartitionSpec as P


KERNEL = 4
SPAN = 256


def from_behind(value, axis, by):
    length = lax.axis_size(axis)
    pairs = [(i, i + by) for i in range(length) if 0 <= i + by < length]
    return lax.ppermute(value, axis, pairs)


def silu_conv(signal, previous_rows, kernel_taps):
    length = signal.shape[0]
    channels = signal.shape[1]
    padded = jnp.concatenate(
        [previous_rows.astype(jnp.float32), signal.astype(jnp.float32)], axis=0
    )
    summed = jnp.zeros((length, channels), jnp.float32) + kernel_taps[KERNEL][None, :]
    for offset in range(KERNEL):
        summed = summed + kernel_taps[offset][None, :] * padded[offset : offset + length]
    return jax.nn.silu(summed).astype(jnp.bfloat16)


def relay_states(decay, state, axis):
    length = lax.axis_size(axis)
    heads = decay.shape[0]
    size = state.size
    pad = (-heads) % 128

    def pack(d, s):
        return jnp.concatenate([s.reshape(-1), jnp.pad(d, (0, pad))])

    def unpack(payload):
        return payload[size : size + heads], payload[:size].reshape(heads, -1)

    flat_state = state.reshape(heads, -1)
    arrived = from_behind(pack(decay, flat_state), axis, 1)
    excl_decay, excl_state = unpack(arrived)
    incl_state = decay[:, None] * excl_state + flat_state
    incl_decay = decay * excl_decay
    shift = 2
    while shift < length:
        sent = from_behind(pack(incl_decay, incl_state), axis, shift)
        got_decay, got_state = unpack(sent)
        excl_state = excl_decay[:, None] * got_state + excl_state
        incl_state = incl_decay[:, None] * got_state + incl_state
        excl_decay = excl_decay * got_decay
        incl_decay = incl_decay * got_decay
        shift *= 2
    return excl_state.reshape(state.shape)


def per_device(inner_tokens, state_inputs, step_raw, conv_inner, conv_state, head_rates, skip_gain):
    x_local, step_local = (
        lax.all_to_all(inner_tokens, "head", split_axis=1, concat_axis=0, tiled=True),
        lax.all_to_all(step_raw, "head", split_axis=1, concat_axis=0, tiled=True),
    )
    context = x_local.shape[0]
    channels = x_local.shape[1]
    heads_local = head_rates.shape[1]
    head_width = channels // heads_local
    margin_rows = KERNEL - 1
    state_whole = lax.all_gather(state_inputs, "head", axis=0, tiled=True)
    edge_rows = jnp.concatenate(
        [x_local[context - margin_rows :], state_whole[context - margin_rows :]], axis=1
    )
    previous_rows = from_behind(edge_rows, "ctx", 1)
    x_previous = previous_rows[:, :channels]
    state_conv = silu_conv(state_whole, previous_rows[:, channels:], conv_state)
    inner_conv = silu_conv(x_local, x_previous, conv_inner)
    state_width = state_conv.shape[1] // 2
    b_rows = state_conv[:, :state_width]
    c_rows = state_conv[:, state_width:]
    step_size = jax.nn.softplus(step_local.astype(jnp.float32) + head_rates[0][None, :])
    log_decay = -step_size * jnp.exp(head_rates[1])[None, :]
    x_heads = inner_conv.reshape(context, heads_local, head_width)
    inputs = (x_heads.astype(jnp.float32) * step_size[:, :, None]).astype(jnp.bfloat16)
    block_count = context // SPAN

    c_blocks = c_rows.reshape(block_count, SPAN, state_width)
    b_blocks = b_rows.reshape(block_count, SPAN, state_width)
    u_blocks = inputs.reshape(block_count, SPAN, heads_local, head_width)
    cumulative = jnp.cumsum(log_decay.reshape(block_count, SPAN, heads_local), axis=1)
    ending = cumulative[:, -1, :]

    weights = jnp.exp(ending[:, None, :] - cumulative)
    scaled = weights[:, :, :, None] * u_blocks.astype(jnp.float32)
    block_states = jnp.einsum(
        "bshp,bsn->bhpn", scaled, b_blocks.astype(jnp.float32), precision=lax.Precision.HIGHEST
    )
    block_decay = jnp.exp(ending)
    entering = []
    running = jnp.zeros_like(block_states[0])
    decay_before = []
    running_decay = jnp.ones_like(block_decay[0])
    for k in range(block_count):
        entering.append(running)
        decay_before.append(running_decay)
        running = block_decay[k][:, None, None] * running + block_states[k]
        running_decay = running_decay * block_decay[k]
    incoming = relay_states(running_decay, running, "ctx")

    inner_scores = jnp.einsum("btn,bsn->bts", c_blocks, b_blocks, preferred_element_type=jnp.float32)
    across = cumulative.transpose(0, 2, 1)
    spread = across[:, :, :, None] - across[:, :, None, :]
    places = jnp.arange(SPAN)
    causal = places[:, None] >= places[None, :]
    mixing = (
        inner_scores[:, None] * jnp.exp(jnp.where(causal[None, None], spread, -jnp.inf))
    ).astype(jnp.bfloat16)
    local_terms = jnp.einsum(
        "bhts,bshp->bthp", mixing, u_blocks, preferred_element_type=jnp.float32
    )
    c_float = c_blocks.astype(jnp.float32)
    entering_intra = jnp.stack(entering).reshape(block_count, channels, state_width)
    carried_intra = jnp.einsum(
        "btn,bkn->btk", c_float, entering_intra, precision=lax.Precision.HIGHEST
    ).reshape(block_count, SPAN, heads_local, head_width)
    decay_in = jnp.exp(cumulative)
    known = (
        local_terms
        + decay_in[:, :, :, None] * carried_intra
        + skip_gain[None, None, :, None] * u_x(x_heads, block_count)
    )

    partial = known.astype(jnp.bfloat16).reshape(context, channels)
    factor = (decay_in * jnp.stack(decay_before)[:, None, :]).reshape(context, heads_local)
    partial_tokens = lax.all_to_all(partial, "head", split_axis=0, concat_axis=1, tiled=True)
    factor_tokens = lax.all_to_all(factor, "head", split_axis=0, concat_axis=1, tiled=True)

    tokens = inner_tokens.shape[0]
    group = lax.axis_index("head")
    c_tokens = lax.dynamic_slice_in_dim(c_rows, group * tokens, tokens, axis=0).astype(jnp.float32)
    incoming_all = lax.all_gather(incoming, "head", axis=0, tiled=True)
    carried_in = jnp.einsum(
        "tn,kn->tk",
        c_tokens,
        incoming_all.reshape(-1, state_width),
        precision=lax.Precision.HIGHEST,
    ).reshape(tokens, factor_tokens.shape[1], head_width)
    summed = partial_tokens.astype(jnp.float32).reshape(carried_in.shape) + (
        factor_tokens[:, :, None] * carried_in
    )
    return summed.astype(jnp.bfloat16).reshape(tokens, -1)


def u_x(x_heads, block_count):
    return x_heads.astype(jnp.float32).reshape(block_count, SPAN, *x_heads.shape[1:])


def solution(mesh):
    return jax.shard_map(
        per_device,
        mesh=mesh,
        in_specs=(
            P(("run", "ctx", "head"), None),
            P(("run", "ctx", "head"), None),
            P(("run", "ctx", "head"), None),
            P(None, "head"),
            P(),
            P("run", "head"),
            P("head"),
        ),
        out_specs=P(("run", "ctx", "head"), None),
        check_vma=False,
    )
```

```python
import jax
import jax.numpy as jnp
from jax import lax
from jax.sharding import PartitionSpec as P


KERNEL = 4
SPAN = 256


def from_behind(value, axis, by):
    length = lax.axis_size(axis)
    pairs = [(i, i + by) for i in range(length) if 0 <= i + by < length]
    return lax.ppermute(value, axis, pairs)


def silu_conv(signal, previous_rows, kernel_taps):
    length = signal.shape[0]
    channels = signal.shape[1]
    padded = jnp.concatenate(
        [previous_rows.astype(jnp.float32), signal.astype(jnp.float32)], axis=0
    )
    summed = jnp.zeros((length, channels), jnp.float32) + kernel_taps[KERNEL][None, :]
    for offset in range(KERNEL):
        summed = summed + kernel_taps[offset][None, :] * padded[offset : offset + length]
    return jax.nn.silu(summed).astype(jnp.bfloat16)


def relay_states(decay, state, axis):
    length = lax.axis_size(axis)
    heads = decay.shape[0]
    size = state.size
    pad = (-heads) % 128

    def pack(d, s):
        return jnp.concatenate([s.reshape(-1), jnp.pad(d, (0, pad))])

    def unpack(payload):
        return payload[size : size + heads], payload[:size].reshape(heads, -1)

    flat_state = state.reshape(heads, -1)
    arrived = from_behind(pack(decay, flat_state), axis, 1)
    excl_decay, excl_state = unpack(arrived)
    incl_state = decay[:, None] * excl_state + flat_state
    incl_decay = decay * excl_decay
    shift = 2
    while shift < length:
        sent = from_behind(pack(incl_decay, incl_state), axis, shift)
        got_decay, got_state = unpack(sent)
        excl_state = excl_decay[:, None] * got_state + excl_state
        incl_state = incl_decay[:, None] * got_state + incl_state
        excl_decay = excl_decay * got_decay
        incl_decay = incl_decay * got_decay
        shift *= 2
    return excl_state.reshape(state.shape)


def per_device(inner_tokens, state_inputs, step_raw, conv_inner, conv_state, head_rates, skip_gain):
    x_local, step_local = (
        lax.all_to_all(inner_tokens, "head", split_axis=1, concat_axis=0, tiled=True),
        lax.all_to_all(step_raw, "head", split_axis=1, concat_axis=0, tiled=True),
    )
    context = x_local.shape[0]
    channels = x_local.shape[1]
    heads_local = head_rates.shape[1]
    head_width = channels // heads_local
    margin_rows = KERNEL - 1
    state_whole = lax.all_gather(state_inputs, "head", axis=0, tiled=True)
    edge_rows = jnp.concatenate(
        [x_local[context - margin_rows :], state_whole[context - margin_rows :]], axis=1
    )
    previous_rows = from_behind(edge_rows, "ctx", 1)
    x_previous = previous_rows[:, :channels]
    state_conv = silu_conv(state_whole, previous_rows[:, channels:], conv_state)
    inner_conv = lax.optimization_barrier(silu_conv(x_local, x_previous, conv_inner))
    state_width = state_conv.shape[1] // 2
    b_rows = state_conv[:, :state_width]
    c_rows = state_conv[:, state_width:]
    step_size = jax.nn.softplus(step_local.astype(jnp.float32) + head_rates[0][None, :])
    log_decay = -step_size * jnp.exp(head_rates[1])[None, :]
    x_heads = inner_conv.reshape(context, heads_local, head_width)
    inputs = (x_heads.astype(jnp.float32) * step_size[:, :, None]).astype(jnp.bfloat16)
    block_count = context // SPAN

    c_blocks = c_rows.reshape(block_count, SPAN, state_width)
    b_blocks = b_rows.reshape(block_count, SPAN, state_width)
    u_blocks = inputs.reshape(block_count, SPAN, heads_local, head_width)
    cumulative = jnp.cumsum(log_decay.reshape(block_count, SPAN, heads_local), axis=1)
    ending = cumulative[:, -1, :]

    weights = jnp.exp(ending[:, None, :] - cumulative)
    scaled = weights[:, :, :, None] * u_blocks.astype(jnp.float32)
    scaled_high = scaled.astype(jnp.bfloat16)
    scaled_low = (scaled - scaled_high.astype(jnp.float32)).astype(jnp.bfloat16)
    block_states = jnp.einsum(
        "bshp,bsn->bhpn",
        jnp.concatenate([scaled_high, scaled_low], axis=1),
        jnp.concatenate([b_blocks, b_blocks], axis=1),
        preferred_element_type=jnp.float32,
    )
    block_decay = jnp.exp(ending)
    entering = []
    running = jnp.zeros_like(block_states[0])
    decay_before = []
    running_decay = jnp.ones_like(block_decay[0])
    for k in range(block_count):
        entering.append(running)
        decay_before.append(running_decay)
        running = block_decay[k][:, None, None] * running + block_states[k]
        running_decay = running_decay * block_decay[k]
    incoming = relay_states(running_decay, running, "ctx")

    inner_scores = jnp.einsum("btn,bsn->bts", c_blocks, b_blocks, preferred_element_type=jnp.float32)
    across = cumulative.transpose(0, 2, 1)
    spread = across[:, :, :, None] - across[:, :, None, :]
    places = jnp.arange(SPAN)
    causal = places[:, None] >= places[None, :]
    mixing = (
        inner_scores[:, None] * jnp.exp(jnp.where(causal[None, None], spread, -jnp.inf))
    ).astype(jnp.bfloat16)
    local_terms = jnp.einsum(
        "bhts,bshp->bthp", mixing, u_blocks, preferred_element_type=jnp.float32
    )
    c_float = c_blocks.astype(jnp.float32)
    entering_intra = jnp.stack(entering).reshape(block_count, channels, state_width)
    carried_intra = jnp.einsum(
        "btn,bkn->btk", c_float, entering_intra, precision=lax.Precision.HIGHEST
    ).reshape(block_count, SPAN, heads_local, head_width)
    decay_in = jnp.exp(cumulative)
    known = (
        local_terms
        + decay_in[:, :, :, None] * carried_intra
        + skip_gain[None, None, :, None] * u_x(x_heads, block_count)
    )

    partial = known.astype(jnp.bfloat16).reshape(context, channels)
    factor = (decay_in * jnp.stack(decay_before)[:, None, :]).reshape(context, heads_local)
    partial_tokens = lax.all_to_all(partial, "head", split_axis=0, concat_axis=1, tiled=True)
    factor_tokens = lax.all_to_all(factor, "head", split_axis=0, concat_axis=1, tiled=True)

    tokens = inner_tokens.shape[0]
    group = lax.axis_index("head")
    c_tokens = lax.dynamic_slice_in_dim(c_rows, group * tokens, tokens, axis=0).astype(jnp.float32)
    incoming_all = lax.all_gather(incoming, "head", axis=0, tiled=True)
    carried_in = jnp.einsum(
        "tn,kn->tk",
        c_tokens,
        incoming_all.reshape(-1, state_width),
        precision=lax.Precision.HIGHEST,
    ).reshape(tokens, factor_tokens.shape[1], head_width)
    summed = partial_tokens.astype(jnp.float32).reshape(carried_in.shape) + (
        factor_tokens[:, :, None] * carried_in
    )
    return summed.astype(jnp.bfloat16).reshape(tokens, -1)


def u_x(x_heads, block_count):
    return x_heads.astype(jnp.float32).reshape(block_count, SPAN, *x_heads.shape[1:])


def solution(mesh):
    return jax.shard_map(
        per_device,
        mesh=mesh,
        in_specs=(
            P(("run", "ctx", "head"), None),
            P(("run", "ctx", "head"), None),
            P(("run", "ctx", "head"), None),
            P(None, "head"),
            P(),
            P("run", "head"),
            P("head"),
        ),
        out_specs=P(("run", "ctx", "head"), None),
        check_vma=False,
    )
```

```python
import jax
import jax.numpy as jnp
from jax import lax
from jax.sharding import PartitionSpec as P


KERNEL = 4
SPAN = 256


def from_behind(value, axis, by):
    length = lax.axis_size(axis)
    pairs = [(i, i + by) for i in range(length) if 0 <= i + by < length]
    return lax.ppermute(value, axis, pairs)


def silu_conv(signal, previous_rows, kernel_taps):
    length = signal.shape[0]
    channels = signal.shape[1]
    padded = jnp.concatenate(
        [previous_rows.astype(jnp.float32), signal.astype(jnp.float32)], axis=0
    )
    summed = jnp.zeros((length, channels), jnp.float32) + kernel_taps[KERNEL][None, :]
    for offset in range(KERNEL):
        summed = summed + kernel_taps[offset][None, :] * padded[offset : offset + length]
    return jax.nn.silu(summed).astype(jnp.bfloat16)


def relay_states(decay, state, axis):
    length = lax.axis_size(axis)
    heads = decay.shape[0]
    size = state.size
    pad = (-heads) % 128

    def pack(d, s):
        return jnp.concatenate([s.reshape(-1), jnp.pad(d, (0, pad))])

    def unpack(payload):
        return payload[size : size + heads], payload[:size].reshape(heads, -1)

    flat_state = state.reshape(heads, -1)
    arrived = from_behind(pack(decay, flat_state), axis, 1)
    excl_decay, excl_state = unpack(arrived)
    incl_state = decay[:, None] * excl_state + flat_state
    incl_decay = decay * excl_decay
    shift = 2
    while shift < length:
        sent = from_behind(pack(incl_decay, incl_state), axis, shift)
        got_decay, got_state = unpack(sent)
        excl_state = excl_decay[:, None] * got_state + excl_state
        incl_state = incl_decay[:, None] * got_state + incl_state
        excl_decay = excl_decay * got_decay
        incl_decay = incl_decay * got_decay
        shift *= 2
    return excl_state.reshape(state.shape)


def per_device(inner_tokens, state_inputs, step_raw, conv_inner, conv_state, head_rates, skip_gain):
    x_local, step_local = (
        lax.all_to_all(inner_tokens, "head", split_axis=1, concat_axis=0, tiled=True),
        lax.all_to_all(step_raw, "head", split_axis=1, concat_axis=0, tiled=True),
    )
    context = x_local.shape[0]
    channels = x_local.shape[1]
    heads_local = head_rates.shape[1]
    head_width = channels // heads_local
    margin_rows = KERNEL - 1
    state_whole = lax.all_to_all(
        jnp.tile(state_inputs, (lax.axis_size("head"), 1)), "head", split_axis=0, concat_axis=0, tiled=True
    )
    edge_rows = jnp.concatenate(
        [x_local[context - margin_rows :], state_whole[context - margin_rows :]], axis=1
    )
    previous_rows = from_behind(edge_rows, "ctx", 1)
    x_previous = previous_rows[:, :channels]
    state_conv = silu_conv(state_whole, previous_rows[:, channels:], conv_state)
    inner_conv = silu_conv(x_local, x_previous, conv_inner)
    state_width = state_conv.shape[1] // 2
    b_rows = state_conv[:, :state_width]
    c_rows = state_conv[:, state_width:]
    step_size = jax.nn.softplus(step_local.astype(jnp.float32) + head_rates[0][None, :])
    log_decay = -step_size * jnp.exp(head_rates[1])[None, :]
    x_heads = inner_conv.reshape(context, heads_local, head_width)
    inputs = (x_heads.astype(jnp.float32) * step_size[:, :, None]).astype(jnp.bfloat16)
    block_count = context // SPAN

    c_blocks = c_rows.reshape(block_count, SPAN, state_width)
    b_blocks = b_rows.reshape(block_count, SPAN, state_width)
    u_blocks = inputs.reshape(block_count, SPAN, heads_local, head_width)
    cumulative = jnp.cumsum(log_decay.reshape(block_count, SPAN, heads_local), axis=1)
    ending = cumulative[:, -1, :]

    weights = jnp.exp(ending[:, None, :] - cumulative)
    scaled = weights[:, :, :, None] * u_blocks.astype(jnp.float32)
    block_states = jnp.einsum(
        "bshp,bsn->bhpn", scaled, b_blocks.astype(jnp.float32), precision=lax.Precision.HIGHEST
    )
    block_decay = jnp.exp(ending)
    entering = []
    running = jnp.zeros_like(block_states[0])
    decay_before = []
    running_decay = jnp.ones_like(block_decay[0])
    for k in range(block_count):
        entering.append(running)
        decay_before.append(running_decay)
        running = block_decay[k][:, None, None] * running + block_states[k]
        running_decay = running_decay * block_decay[k]
    incoming = relay_states(running_decay, running, "ctx")

    inner_scores = jnp.einsum("btn,bsn->bts", c_blocks, b_blocks, preferred_element_type=jnp.float32)
    across = cumulative.transpose(0, 2, 1)
    spread = across[:, :, :, None] - across[:, :, None, :]
    places = jnp.arange(SPAN)
    causal = places[:, None] >= places[None, :]
    mixing = (
        inner_scores[:, None] * jnp.exp(jnp.where(causal[None, None], spread, -jnp.inf))
    ).astype(jnp.bfloat16)
    local_terms = jnp.einsum(
        "bhts,bshp->bthp", mixing, u_blocks, preferred_element_type=jnp.float32
    )
    c_float = c_blocks.astype(jnp.float32)
    entering_intra = jnp.stack(entering).reshape(block_count, channels, state_width)
    carried_intra = jnp.einsum(
        "btn,bkn->btk", c_float, entering_intra, precision=lax.Precision.HIGHEST
    ).reshape(block_count, SPAN, heads_local, head_width)
    decay_in = jnp.exp(cumulative)
    known = (
        local_terms
        + decay_in[:, :, :, None] * carried_intra
        + skip_gain[None, None, :, None] * u_x(x_heads, block_count)
    )

    partial = known.astype(jnp.bfloat16).reshape(context, channels)
    factor = (decay_in * jnp.stack(decay_before)[:, None, :]).reshape(context, heads_local)
    partial_tokens = lax.all_to_all(partial, "head", split_axis=0, concat_axis=1, tiled=True)
    factor_tokens = lax.all_to_all(factor, "head", split_axis=0, concat_axis=1, tiled=True)

    tokens = inner_tokens.shape[0]
    group = lax.axis_index("head")
    c_tokens = lax.dynamic_slice_in_dim(c_rows, group * tokens, tokens, axis=0).astype(jnp.float32)
    groups = lax.axis_size("head")
    incoming_all = lax.all_to_all(
        jnp.tile(incoming, (groups, 1, 1)), "head", split_axis=0, concat_axis=0, tiled=True
    )
    carried_in = jnp.einsum(
        "tn,kn->tk",
        c_tokens,
        incoming_all.reshape(-1, state_width),
        precision=lax.Precision.HIGHEST,
    ).reshape(tokens, factor_tokens.shape[1], head_width)
    summed = partial_tokens.astype(jnp.float32).reshape(carried_in.shape) + (
        factor_tokens[:, :, None] * carried_in
    )
    return summed.astype(jnp.bfloat16).reshape(tokens, -1)


def u_x(x_heads, block_count):
    return x_heads.astype(jnp.float32).reshape(block_count, SPAN, *x_heads.shape[1:])


def solution(mesh):
    return jax.shard_map(
        per_device,
        mesh=mesh,
        in_specs=(
            P(("run", "ctx", "head"), None),
            P(("run", "ctx", "head"), None),
            P(("run", "ctx", "head"), None),
            P(None, "head"),
            P(),
            P("run", "head"),
            P("head"),
        ),
        out_specs=P(("run", "ctx", "head"), None),
        check_vma=False,
    )
```

```python
import jax
import jax.numpy as jnp
from jax import lax
from jax.sharding import PartitionSpec as P


KERNEL = 4
SPAN = 256


def from_behind(value, axis, by):
    length = lax.axis_size(axis)
    pairs = [(i, i + by) for i in range(length) if 0 <= i + by < length]
    return lax.ppermute(value, axis, pairs)


def silu_conv(signal, previous_rows, kernel_taps):
    length = signal.shape[0]
    channels = signal.shape[1]
    padded = jnp.concatenate(
        [previous_rows.astype(jnp.float32), signal.astype(jnp.float32)], axis=0
    )
    summed = jnp.zeros((length, channels), jnp.float32) + kernel_taps[KERNEL][None, :]
    for offset in range(KERNEL):
        summed = summed + kernel_taps[offset][None, :] * padded[offset : offset + length]
    return jax.nn.silu(summed).astype(jnp.bfloat16)


def relay_states(decay, state, axis):
    length = lax.axis_size(axis)
    heads = decay.shape[0]
    size = state.size
    pad = (-heads) % 128

    def pack(d, s):
        return jnp.concatenate([s.reshape(-1), jnp.pad(d, (0, pad))])

    def unpack(payload):
        return payload[size : size + heads], payload[:size].reshape(heads, -1)

    flat_state = state.reshape(heads, -1)
    arrived = from_behind(pack(decay, flat_state), axis, 1)
    excl_decay, excl_state = unpack(arrived)
    incl_state = decay[:, None] * excl_state + flat_state
    incl_decay = decay * excl_decay
    shift = 2
    while shift < length:
        sent = from_behind(pack(incl_decay, incl_state), axis, shift)
        got_decay, got_state = unpack(sent)
        excl_state = excl_decay[:, None] * got_state + excl_state
        incl_state = incl_decay[:, None] * got_state + incl_state
        excl_decay = excl_decay * got_decay
        incl_decay = incl_decay * got_decay
        shift *= 2
    return excl_state.reshape(state.shape)


def per_device(inner_tokens, state_inputs, step_raw, conv_inner, conv_state, head_rates, skip_gain):
    x_local = lax.all_to_all(inner_tokens, "head", split_axis=1, concat_axis=0, tiled=True)
    groups = lax.axis_size("head")
    rows = inner_tokens.shape[0]
    step_chunks = step_raw.reshape(rows, groups, -1).transpose(1, 0, 2).reshape(groups * rows, -1)
    shared = lax.all_to_all(
        jnp.concatenate([jnp.tile(state_inputs, (groups, 1)), step_chunks], axis=1),
        "head", split_axis=0, concat_axis=0, tiled=True,
    )
    state_whole = shared[:, : state_inputs.shape[1]]
    step_local = shared[:, state_inputs.shape[1] :]
    context = x_local.shape[0]
    channels = x_local.shape[1]
    heads_local = head_rates.shape[1]
    head_width = channels // heads_local
    margin_rows = KERNEL - 1
    edge_rows = jnp.concatenate(
        [x_local[context - margin_rows :], state_whole[context - margin_rows :]], axis=1
    )
    previous_rows = from_behind(edge_rows, "ctx", 1)
    x_previous = previous_rows[:, :channels]
    state_conv = silu_conv(state_whole, previous_rows[:, channels:], conv_state)
    inner_conv = silu_conv(x_local, x_previous, conv_inner)
    state_width = state_conv.shape[1] // 2
    b_rows = state_conv[:, :state_width]
    c_rows = state_conv[:, state_width:]
    step_size = jax.nn.softplus(step_local.astype(jnp.float32) + head_rates[0][None, :])
    log_decay = -step_size * jnp.exp(head_rates[1])[None, :]
    x_heads = inner_conv.reshape(context, heads_local, head_width)
    inputs = (x_heads.astype(jnp.float32) * step_size[:, :, None]).astype(jnp.bfloat16)
    block_count = context // SPAN

    c_blocks = c_rows.reshape(block_count, SPAN, state_width)
    b_blocks = b_rows.reshape(block_count, SPAN, state_width)
    u_blocks = inputs.reshape(block_count, SPAN, heads_local, head_width)
    cumulative = jnp.cumsum(log_decay.reshape(block_count, SPAN, heads_local), axis=1)
    ending = cumulative[:, -1, :]

    weights = jnp.exp(ending[:, None, :] - cumulative)
    scaled = weights[:, :, :, None] * u_blocks.astype(jnp.float32)
    block_states = jnp.einsum(
        "bshp,bsn->bhpn", scaled, b_blocks.astype(jnp.float32), precision=lax.Precision.HIGHEST
    )
    block_decay = jnp.exp(ending)
    entering = []
    running = jnp.zeros_like(block_states[0])
    decay_before = []
    running_decay = jnp.ones_like(block_decay[0])
    for k in range(block_count):
        entering.append(running)
        decay_before.append(running_decay)
        running = block_decay[k][:, None, None] * running + block_states[k]
        running_decay = running_decay * block_decay[k]
    incoming = relay_states(running_decay, running, "ctx")

    inner_scores = jnp.einsum("btn,bsn->bts", c_blocks, b_blocks, preferred_element_type=jnp.float32)
    across = cumulative.transpose(0, 2, 1)
    spread = across[:, :, :, None] - across[:, :, None, :]
    places = jnp.arange(SPAN)
    causal = places[:, None] >= places[None, :]
    mixing = (
        inner_scores[:, None] * jnp.exp(jnp.where(causal[None, None], spread, -jnp.inf))
    ).astype(jnp.bfloat16)
    local_terms = jnp.einsum(
        "bhts,bshp->bthp", mixing, u_blocks, preferred_element_type=jnp.float32
    )
    c_float = c_blocks.astype(jnp.float32)
    entering_intra = jnp.stack(entering).reshape(block_count, channels, state_width)
    carried_intra = jnp.einsum(
        "btn,bkn->btk", c_float, entering_intra, precision=lax.Precision.HIGHEST
    ).reshape(block_count, SPAN, heads_local, head_width)
    decay_in = jnp.exp(cumulative)
    known = (
        local_terms
        + decay_in[:, :, :, None] * carried_intra
        + skip_gain[None, None, :, None] * u_x(x_heads, block_count)
    )

    partial = known.astype(jnp.bfloat16).reshape(context, channels)
    factor = (decay_in * jnp.stack(decay_before)[:, None, :]).reshape(context, heads_local)
    partial_tokens = lax.all_to_all(partial, "head", split_axis=0, concat_axis=1, tiled=True)
    factor_tokens = lax.all_to_all(factor, "head", split_axis=0, concat_axis=1, tiled=True)

    tokens = inner_tokens.shape[0]
    group = lax.axis_index("head")
    c_tokens = lax.dynamic_slice_in_dim(c_rows, group * tokens, tokens, axis=0).astype(jnp.float32)
    incoming_all = lax.all_to_all(
        jnp.tile(incoming, (groups, 1, 1)), "head", split_axis=0, concat_axis=0, tiled=True
    )
    carried_in = jnp.einsum(
        "tn,kn->tk",
        c_tokens,
        incoming_all.reshape(-1, state_width),
        precision=lax.Precision.HIGHEST,
    ).reshape(tokens, factor_tokens.shape[1], head_width)
    summed = partial_tokens.astype(jnp.float32).reshape(carried_in.shape) + (
        factor_tokens[:, :, None] * carried_in
    )
    return summed.astype(jnp.bfloat16).reshape(tokens, -1)


def u_x(x_heads, block_count):
    return x_heads.astype(jnp.float32).reshape(block_count, SPAN, *x_heads.shape[1:])


def solution(mesh):
    return jax.shard_map(
        per_device,
        mesh=mesh,
        in_specs=(
            P(("run", "ctx", "head"), None),
            P(("run", "ctx", "head"), None),
            P(("run", "ctx", "head"), None),
            P(None, "head"),
            P(),
            P("run", "head"),
            P("head"),
        ),
        out_specs=P(("run", "ctx", "head"), None),
        check_vma=False,
    )
```
